256 devices in a mesh: orb: 8 (over z_lo, core), box: 32 (over x, y, z_hi).
Axes of the slice: x: 4, y: 4, z: 8 (z_hi: 2, z_lo: 4; z = z_hi * 4 + z_lo), core: 2. Of those that a mesh axis runs over, the one named last changes fastest.
Arguments:
- orbitals: bfloat16 [768, 256, 1000], P('orb', 'box'), may hold values from -6 to 6
- exchange_values: bfloat16 [768, 256, 1000], P('orb', 'box'), may hold values from -6 to 6
- local_values: float32 [256, 1000], P('box'), may hold values from -6 to 6
- coupling: bfloat16 [768, 768], P('orb'), may hold values from -0.21875 to 0.21875
- to_values_mat: float32 [10, 10], replicated, may hold values from -2 to 2
- to_coeffs_mat: float32 [10, 10], replicated, may hold values from -2 to 2
- laplace_blocks: float32 [3, 10, 10], replicated, may hold values from -2 to 2
- box_counts: int32 [32], P('box'), may hold values from 2 to 8, as said below
- kept_mask: int32 [256], P('box'), may hold values from 0 to 1, as said below
- send_list: int32 [32, 32], P('box'), may hold values from -1 to 7, as said below
- neighbour_pos: int32 [6, 256], P(None, 'box'), may hold values from -1 to 39, as said below
Outputs:
- h_orbitals: bfloat16 [768, 256, 1000], P('orb', 'box')
The draws below stay inside these ranges and needn't reach their ends.
Inputs may be any that keep to these rules, and one draw needn't show every extreme that they name: Device d of box holds live boxes in slots 0 to box_counts[d] - 1 of its 8; some device holds 8. `kept_mask`: 1 only on live boxes; at most 4 ones in one device's range, and exactly 4 in some device's range. `send_list`: row q, entries p * 1 to p + 1 - 1: live slots of device q's range passed to device p, -1 for an empty entry; nothing to its own device; at most 1 to one device, exactly 1 to the devices whose index differs by one. `neighbour_pos`: -1: no neighbour; below 8: a live slot of the same device; otherwise the entry of send_list named in the reference program, which is never -1. Boxes that are not live have -1 on every face.
All inputs are finite; a program needn't handle non-finite values.
Results may differ from the reference program's by a relative error of at most 0.0031.
Values may be sent and summed in bfloat16 or wider, within the bound.
No kernel may reach another device: no remote copies, remote signals or barrier semaphores. Data moves between devices by JAX's collectives and lax.ppermute only.
A program may use at most 256 MiB of HBM per device.

```python
import jax
import jax.numpy as jnp
from jax import lax

K = 10
COEF = 1000
ORBITALS = 768
ORB_DEV = 96
BOX_DEV = 8
BOXES = 256
CAP = 1
KEEP = 4
N_BOX = 32


def build_layout(key):
    keys = jax.random.split(jax.random.fold_in(key, 11), 9)
    devices = BOXES // BOX_DEV
    dev_ids = jnp.arange(devices, dtype=jnp.int32)
    counts = jax.random.randint(keys[0], (devices,), BOX_DEV // 4, BOX_DEV + 1)
    fullest = jax.random.randint(keys[1], (), 0, devices)
    counts = jnp.where(dev_ids == fullest, BOX_DEV, counts).astype(jnp.int32)
    spread = jax.random.randint(keys[2], (devices, devices), 0, CAP + 1)
    distance = jnp.abs(dev_ids[:, None] - dev_ids[None, :])
    sent = jnp.where(distance == 1, CAP, spread)
    sent = jnp.where(distance == 0, 0, sent)
    positions = jnp.arange(CAP, dtype=jnp.int32)
    used = positions[None, None, :] < sent[:, :, None]
    chosen = jax.random.randint(keys[3], (devices, devices, CAP), 0, BOX_DEV) % counts[:, None, None]
    send_list = jnp.where(used, chosen, -1).reshape(devices, devices * CAP).astype(jnp.int32)
    arrive = jnp.transpose(used, (1, 0, 2)).reshape(devices, devices * CAP).astype(jnp.int32)
    arrived = jnp.sum(arrive, axis=1)
    running = jnp.cumsum(arrive, axis=1)
    kinds = jax.random.randint(keys[4], (6, devices, BOX_DEV), 0, 10)
    local_pick = jax.random.randint(keys[5], (6, devices, BOX_DEV), 0, BOX_DEV) % counts[None, :, None]
    ranks = jax.random.randint(keys[6], (6, devices, BOX_DEV), 0, 1 << 20) % arrived[None, :, None]
    remote_pick = jnp.sum((running[None, :, None, :] <= ranks[..., None]).astype(jnp.int32), axis=-1)
    faces = jnp.where(kinds == 0, -1, jnp.where(kinds <= 2, local_pick, BOX_DEV + remote_pick))
    slot_ids = jnp.arange(BOX_DEV, dtype=jnp.int32)
    live = slot_ids[None, :] < counts[:, None]
    faces = jnp.where(live[None, :, :], faces, -1).reshape(6, devices * BOX_DEV).astype(jnp.int32)
    quota = jnp.minimum(counts, jax.random.randint(keys[7], (devices,), KEEP // 4, KEEP + 1))
    quota = jnp.where(dev_ids == fullest, KEEP, quota)
    scores = jax.random.randint(keys[8], (devices, BOX_DEV), 0, 1 << 16) * BOX_DEV + slot_ids[None, :]
    scores = jnp.where(live, scores, (1 << 16) * BOX_DEV + slot_ids[None, :])
    order = jnp.argsort(scores, axis=1)
    place = jnp.argsort(order, axis=1)
    kept = (place < quota[:, None]).astype(jnp.int32).reshape(devices * BOX_DEV)
    return (counts, kept, send_list, faces)


def draw_box_counts(key, part):
    return build_layout(key)[0]


def draw_kept_mask(key, part):
    return build_layout(key)[1]


def draw_send_list(key, part):
    return build_layout(key)[2]


def draw_neighbour_pos(key, part):
    return build_layout(key)[3]


def steps_of(own_key, dims, cuts, low, top_value):
    def one(dim, parts):
        steps = jax.random.uniform(jax.random.fold_in(jax.random.fold_in(own_key, 6), dim), (parts,), jnp.float32, low / len(cuts), top_value / len(cuts))
        return jnp.repeat(jnp.exp(steps), dims[dim] // parts).reshape((-1,) + (1,) * (len(dims) - dim - 1))

    level = one(*cuts[0])
    for cut in cuts[1:]:
        level = level * one(*cut)
    return level


def bell_draw(own_key, shape, scale, reach, cuts=(), kind=jnp.bfloat16):
    values = jax.random.normal(own_key, shape, jnp.float32) * scale
    if len(cuts) > 0:
        values = steps_of(own_key, shape, cuts, -0.22, 0.18) * values
    return jnp.clip(values, min=-reach, max=reach).astype(kind)


def setup_inputs(seed: int = 0) -> dict:
    arg_keys = jax.random.split(jax.random.key(seed), 12)
    return {
        "orbitals": bell_draw(arg_keys[0], (ORBITALS, BOXES, COEF), 1.0, 6.0, ((0, 8), (1, 32))),
        "exchange_values": bell_draw(arg_keys[1], (ORBITALS, BOXES, COEF), 1.0, 6.0, ((0, 8), (1, 32))),
        "local_values": bell_draw(arg_keys[2], (BOXES, COEF), 1.0, 6.0, ((0, 32),), jnp.float32),
        "coupling": bell_draw(arg_keys[3], (ORBITALS, ORBITALS), ORBITALS ** -0.5, 0.21875, ((0, 8),)),
        "to_values_mat": bell_draw(arg_keys[4], (K, K), K ** -0.5, 2.0, (), jnp.float32),
        "to_coeffs_mat": bell_draw(arg_keys[5], (K, K), K ** -0.5, 2.0, (), jnp.float32),
        "laplace_blocks": bell_draw(arg_keys[6], (3, K, K), K ** -0.5, 2.0, (), jnp.float32),
        "box_counts": draw_box_counts(jax.random.fold_in(arg_keys[11], 71), 0),
        "kept_mask": draw_kept_mask(jax.random.fold_in(arg_keys[11], 71), 0),
        "send_list": draw_send_list(jax.random.fold_in(arg_keys[11], 71), 0),
        "neighbour_pos": draw_neighbour_pos(jax.random.fold_in(arg_keys[11], 71), 0),
    }


def along_axis(field, matrix, which):
    forms = ("ax,nxbc->nabc", "bx,naxc->nabc", "cx,nabx->nabc")
    return jnp.einsum(forms[which], matrix, field, precision=lax.Precision.HIGHEST)


def three_way(field, matrix):
    result = along_axis(field, matrix, 0)
    result = along_axis(result, matrix, 1)
    return along_axis(result, matrix, 2)


def neighbour_index(send_list, neighbour_pos):
    boxes_all = neighbour_pos.shape[1]
    owner = (jnp.arange(boxes_all, dtype=jnp.int32) // BOX_DEV)[None, :]
    remote = neighbour_pos - BOX_DEV
    source = jnp.clip(remote // CAP, 0, N_BOX - 1).astype(jnp.int32)
    within = (jnp.maximum(remote, 0) % CAP).astype(jnp.int32)
    column = (owner * CAP + within).astype(jnp.int32)
    slot = send_list[source, column]
    remote_global = source * BOX_DEV + slot
    local_global = owner * BOX_DEV + neighbour_pos
    chosen = jnp.where(neighbour_pos < BOX_DEV, local_global, remote_global)
    return jnp.where(neighbour_pos < 0, -1, chosen).astype(jnp.int32)


def reference(orbitals, exchange_values, local_values, coupling, to_values_mat, to_coeffs_mat, laplace_blocks, box_counts, kept_mask, send_list, neighbour_pos):
    global_index = neighbour_index(send_list, neighbour_pos)
    present = global_index >= 0
    safe_index = jnp.maximum(global_index, 0).astype(jnp.int32)
    slot_of = jnp.arange(BOXES, dtype=jnp.int32) % BOX_DEV
    live = slot_of < jnp.repeat(box_counts, BOX_DEV)
    kept = kept_mask > 0
    groups = ORBITALS // ORB_DEV
    cells = (-1, K, K, K)

    def to_values(block):
        shaped = block.astype(jnp.float32).reshape(cells)
        return three_way(shaped, to_values_mat).reshape(block.shape)

    def product_block(pair):
        block, potential = pair
        values = to_values(block)
        weighted = jnp.where(kept[None, :, None], potential.astype(jnp.float32) * values, jnp.float32(0.0))
        return weighted.astype(jnp.bfloat16)

    orbital_blocks = orbitals.reshape(groups, ORB_DEV, BOXES, COEF)
    potential_blocks = exchange_values.reshape(groups, ORB_DEV, BOXES, COEF)
    products = lax.map(product_block, (orbital_blocks, potential_blocks))
    flat_products = products.reshape(ORBITALS, BOXES * COEF)
    coupling_blocks = coupling.reshape(groups, ORB_DEV, ORBITALS)

    def apply_block(pair):
        block, rows = pair
        values = to_values(block)
        exchange = jnp.dot(rows, flat_products, preferred_element_type=jnp.float32).reshape(ORB_DEV, BOXES, COEF)
        weighted = local_values[None, :, :] * values - exchange
        potential_part = three_way(weighted.reshape(cells), to_coeffs_mat)
        center = block.astype(jnp.float32).reshape(cells)
        kinetic = jnp.zeros_like(center)
        for which in range(3):
            kinetic = kinetic + along_axis(center, laplace_blocks[0], which)
            for side in range(2):
                face = 2 * which + side
                moved = jnp.take(block, safe_index[face], axis=1)
                moved = jnp.where(present[face][None, :, None], moved, jnp.zeros_like(moved))
                moved = moved.astype(jnp.float32).reshape(cells)
                kinetic = kinetic + along_axis(moved, laplace_blocks[1 + side], which)
        total = (potential_part - 0.5 * kinetic).reshape(ORB_DEV, BOXES, COEF)
        total = jnp.where(live[None, :, None], total, jnp.float32(0.0))
        return total.astype(jnp.bfloat16)

    result = lax.map(apply_block, (orbital_blocks, coupling_blocks))
    return result.reshape(ORBITALS, BOXES, COEF)
```

```python
import jax
import jax.numpy as jnp
from jax import lax
from jax.sharding import PartitionSpec as P

KEEP = 4


def digit_of(width, order_k, place):
    idx = lax.iota(jnp.int32, width)
    return (idx // (order_k ** (2 - place))) % order_k


def expand(mat, width, place):
    order_k = mat.shape[0]
    digit = digit_of(width, order_k, place)
    ks = lax.iota(jnp.int32, order_k)
    left = (digit[:, None] == ks[None, :]).astype(jnp.float32)
    right = (ks[:, None] == digit[None, :]).astype(jnp.float32)
    hp = lax.Precision.HIGHEST
    return jnp.dot(jnp.dot(left, mat, precision=hp), right, precision=hp)


def same_digit(width, order_k, place):
    digit = digit_of(width, order_k, place)
    return (digit[:, None] == digit[None, :]).astype(jnp.float32)


def kron3(a, b, c):
    width = a.shape[0] * b.shape[0] * c.shape[0]
    return expand(a, width, 0) * expand(b, width, 1) * expand(c, width, 2)


def at_place(mat, width, place):
    order_k = mat.shape[0]
    out = expand(mat, width, place)
    for other in range(3):
        if other != place:
            out = out * same_digit(width, order_k, other)
    return out


def split_bf16(mat):
    hi = lax.reduce_precision(mat, exponent_bits=8, mantissa_bits=7)
    lo = (mat - hi).astype(jnp.bfloat16)
    return hi.astype(jnp.bfloat16), lo


def dot_f32(a, b):
    return jnp.dot(a, b, preferred_element_type=jnp.float32)


def apply_bf16(rows, parts):
    hi, lo = parts
    return dot_f32(rows, hi) + dot_f32(rows, lo)


def apply_f32(rows, parts):
    hi, lo = parts
    rows_hi_f = lax.reduce_precision(rows, exponent_bits=8, mantissa_bits=7)
    rows_lo = (rows - rows_hi_f).astype(jnp.bfloat16)
    rows_hi = rows_hi_f.astype(jnp.bfloat16)
    return dot_f32(rows_hi, hi) + dot_f32(rows_hi, lo) + dot_f32(rows_lo, hi)


def pick(onehot, block):
    return jnp.einsum(
        "sb,nbc->nsc", onehot, block, preferred_element_type=jnp.float32
    ).astype(jnp.bfloat16)


def shards(
    orbitals,
    exchange_values,
    local_values,
    coupling,
    to_values_mat,
    to_coeffs_mat,
    laplace_blocks,
    box_counts,
    kept_mask,
    send_list,
    neighbour_pos,
):
    orb_dev, box_dev, width = orbitals.shape
    order_k = to_values_mat.shape[0]
    n_box = send_list.shape[1]
    rows = orb_dev * box_dev

    slots = send_list[0]
    box_ids = lax.iota(jnp.int32, box_dev)
    send_hot = (slots[:, None] == box_ids[None, :]).astype(jnp.bfloat16)
    outgoing = pick(send_hot, orbitals)
    incoming = lax.all_to_all(outgoing, "box", split_axis=1, concat_axis=1, tiled=True)

    values_t = split_bf16(kron3(to_values_mat, to_values_mat, to_values_mat).T)
    flat = orbitals.reshape(rows, width)
    values = apply_bf16(flat, values_t).reshape(orb_dev, box_dev, width)

    kept = kept_mask > 0
    rank = jnp.cumsum(kept.astype(jnp.int32)) - 1
    keep_ids = lax.iota(jnp.int32, KEEP)
    sel = kept[None, :] & (rank[None, :] == keep_ids[:, None])
    products = jnp.where(
        kept[None, :, None], exchange_values.astype(jnp.float32) * values, 0.0
    ).astype(jnp.bfloat16)
    compact = pick(sel.astype(jnp.bfloat16), products)
    gathered = lax.all_gather(
        compact.reshape(orb_dev, KEEP * width), "orb", axis=0, tiled=True
    )
    mixed = dot_f32(coupling, gathered).reshape(orb_dev, KEEP, width)
    self_f = sel.astype(jnp.float32)
    exchange = mixed[:, 0:1, :] * self_f[0][None, :, None]
    for k in range(1, KEEP):
        exchange = exchange + mixed[:, k : k + 1, :] * self_f[k][None, :, None]

    weighted = local_values[None, :, :] * values - exchange
    coeffs_t = split_bf16(kron3(to_coeffs_mat, to_coeffs_mat, to_coeffs_mat).T)
    potential = apply_f32(weighted.reshape(rows, width), coeffs_t)

    lap0 = laplace_blocks[0]
    centre = sum(at_place(lap0, width, place) for place in range(3))
    kinetic = apply_bf16(flat, split_bf16(centre.T))
    remote_ids = lax.iota(jnp.int32, n_box)
    for which in range(3):
        for side in range(2):
            face_pos = neighbour_pos[2 * which + side]
            local_hot = (face_pos[:, None] == box_ids[None, :]).astype(jnp.bfloat16)
            remote_hot = ((face_pos[:, None] - box_dev) == remote_ids[None, :]).astype(
                jnp.bfloat16
            )
            moved = pick(local_hot, orbitals) + pick(remote_hot, incoming)
            face_mat = at_place(laplace_blocks[1 + side], width, which)
            kinetic = kinetic + apply_bf16(
                moved.reshape(rows, width), split_bf16(face_mat.T)
            )

    total = (potential - 0.5 * kinetic).reshape(orb_dev, box_dev, width)
    live = box_ids < box_counts[0]
    total = jnp.where(live[None, :, None], total, 0.0)
    return total.astype(jnp.bfloat16)


def solution(mesh):
    return jax.shard_map(
        shards,
        mesh=mesh,
        in_specs=(
            P("orb", "box", None),
            P("orb", "box", None),
            P("box", None),
            P("orb", None),
            P(),
            P(),
            P(),
            P("box"),
            P("box"),
            P("box", None),
            P(None, "box"),
        ),
        out_specs=P("orb", "box", None),
        check_vma=False,
    )
```

```python
import jax
import jax.numpy as jnp
from jax import lax
from jax.sharding import PartitionSpec as P

KEEP = 4


def digit_of(width, order_k, place):
    idx = lax.iota(jnp.int32, width)
    return (idx // (order_k ** (2 - place))) % order_k


def expand(mat, width, place):
    order_k = mat.shape[0]
    digit = digit_of(width, order_k, place)
    ks = lax.iota(jnp.int32, order_k)
    left = (digit[:, None] == ks[None, :]).astype(jnp.float32)
    right = (ks[:, None] == digit[None, :]).astype(jnp.float32)
    hp = lax.Precision.HIGHEST
    return jnp.dot(jnp.dot(left, mat, precision=hp), right, precision=hp)


def same_digit(width, order_k, place):
    digit = digit_of(width, order_k, place)
    return (digit[:, None] == digit[None, :]).astype(jnp.float32)


def kron3(a, b, c):
    width = a.shape[0] * b.shape[0] * c.shape[0]
    return expand(a, width, 0) * expand(b, width, 1) * expand(c, width, 2)


def at_place(mat, width, place):
    order_k = mat.shape[0]
    out = expand(mat, width, place)
    for other in range(3):
        if other != place:
            out = out * same_digit(width, order_k, other)
    return out


def split_bf16(mat):
    hi = lax.reduce_precision(mat, exponent_bits=8, mantissa_bits=7)
    lo = (mat - hi).astype(jnp.bfloat16)
    return hi.astype(jnp.bfloat16), lo


def dot_f32(a, b):
    return jnp.dot(a, b, preferred_element_type=jnp.float32)


def apply_bf16(rows, parts):
    hi, lo = parts
    return dot_f32(rows, hi) + dot_f32(rows, lo)


def apply_f32(rows, parts):
    hi, lo = parts
    rows_hi_f = lax.reduce_precision(rows, exponent_bits=8, mantissa_bits=7)
    rows_lo = (rows - rows_hi_f).astype(jnp.bfloat16)
    rows_hi = rows_hi_f.astype(jnp.bfloat16)
    return dot_f32(rows_hi, hi) + dot_f32(rows_hi, lo) + dot_f32(rows_lo, hi)


def pick(onehot, block):
    return jnp.einsum(
        "sb,nbc->nsc", onehot, block, preferred_element_type=jnp.float32
    ).astype(jnp.bfloat16)


def shards(
    orbitals,
    exchange_values,
    local_values,
    coupling,
    to_values_mat,
    to_coeffs_mat,
    laplace_blocks,
    box_counts,
    kept_mask,
    send_list,
    neighbour_pos,
):
    orb_dev, box_dev, width = orbitals.shape
    order_k = to_values_mat.shape[0]
    n_box = send_list.shape[1]
    rows = orb_dev * box_dev

    slots = send_list[0]
    box_ids = lax.iota(jnp.int32, box_dev)
    send_hot = (slots[:, None] == box_ids[None, :]).astype(jnp.bfloat16)
    outgoing = pick(send_hot, orbitals)
    incoming = lax.all_to_all(outgoing, "box", split_axis=1, concat_axis=1, tiled=True)

    values_t = split_bf16(kron3(to_values_mat, to_values_mat, to_values_mat).T)
    flat = orbitals.reshape(rows, width)
    values = apply_bf16(flat, values_t).reshape(orb_dev, box_dev, width)

    kept = kept_mask > 0
    rank = jnp.cumsum(kept.astype(jnp.int32)) - 1
    keep_ids = lax.iota(jnp.int32, KEEP)
    sel = kept[None, :] & (rank[None, :] == keep_ids[:, None])
    products = jnp.where(
        kept[None, :, None], exchange_values.astype(jnp.float32) * values, 0.0
    ).astype(jnp.bfloat16)
    compact = pick(sel.astype(jnp.bfloat16), products)
    gathered = lax.all_gather(
        compact.reshape(orb_dev, KEEP * width), "orb", axis=0, tiled=True
    )
    lap0 = laplace_blocks[0]
    centre = sum(at_place(lap0, width, place) for place in range(3))
    kinetic = apply_bf16(flat, split_bf16(centre.T))
    faces = [at_place(laplace_blocks[1 + side], width, which).T
             for which in range(3) for side in range(2)]
    face_hi, face_lo = split_bf16(jnp.stack(faces))
    pool = jnp.concatenate([orbitals, incoming], axis=1)
    pool_ids = lax.iota(jnp.int32, pool.shape[1])
    face_pos = neighbour_pos.reshape(-1)
    face_hot = (face_pos[:, None] == pool_ids[None, :]).astype(jnp.bfloat16)
    moved = pick(face_hot, pool).reshape(orb_dev, len(faces), box_dev, width)
    kinetic_faces = jnp.einsum(
        "nfbc,fcd->nbd", moved, face_hi, preferred_element_type=jnp.float32
    ) + jnp.einsum("nfbc,fcd->nbd", moved, face_lo, preferred_element_type=jnp.float32)
    kinetic = kinetic + kinetic_faces.reshape(rows, width)
    gathered, kinetic = lax.optimization_barrier((gathered, kinetic))
    mixed = dot_f32(coupling, gathered).reshape(orb_dev, KEEP, width)
    spread = jnp.take(mixed, jnp.clip(rank, 0, KEEP - 1), axis=1)
    exchange = jnp.where(kept[None, :, None], spread, 0.0)

    weighted = local_values[None, :, :] * values - exchange
    coeffs_t = split_bf16(kron3(to_coeffs_mat, to_coeffs_mat, to_coeffs_mat).T)
    potential = apply_f32(weighted.reshape(rows, width), coeffs_t)

    total = (potential - 0.5 * kinetic).reshape(orb_dev, box_dev, width)
    live = box_ids < box_counts[0]
    total = jnp.where(live[None, :, None], total, 0.0)
    return total.astype(jnp.bfloat16)


def solution(mesh):
    return jax.shard_map(
        shards,
        mesh=mesh,
        in_specs=(
            P("orb", "box", None),
            P("orb", "box", None),
            P("box", None),
            P("orb", None),
            P(),
            P(),
            P(),
            P("box"),
            P("box"),
            P("box", None),
            P(None, "box"),
        ),
        out_specs=P("orb", "box", None),
        check_vma=False,
    )
```

```python
import jax
import jax.numpy as jnp
from jax import lax
from jax.sharding import PartitionSpec as P

KEEP = 4


def digit_of(width, order_k, place):
    idx = lax.iota(jnp.int32, width)
    return (idx // (order_k ** (2 - place))) % order_k


def expand(mat, width, place):
    order_k = mat.shape[0]
    digit = digit_of(width, order_k, place)
    ks = lax.iota(jnp.int32, order_k)
    left = (digit[:, None] == ks[None, :]).astype(jnp.float32)
    right = (ks[:, None] == digit[None, :]).astype(jnp.float32)
    hp = lax.Precision.HIGHEST
    return jnp.dot(jnp.dot(left, mat, precision=hp), right, precision=hp)


def same_digit(width, order_k, place):
    digit = digit_of(width, order_k, place)
    return (digit[:, None] == digit[None, :]).astype(jnp.float32)


def kron3(a, b, c):
    width = a.shape[0] * b.shape[0] * c.shape[0]
    return expand(a, width, 0) * expand(b, width, 1) * expand(c, width, 2)


def at_place(mat, width, place):
    order_k = mat.shape[0]
    out = expand(mat, width, place)
    for other in range(3):
        if other != place:
            out = out * same_digit(width, order_k, other)
    return out


def split_bf16(mat):
    hi = lax.reduce_precision(mat, exponent_bits=8, mantissa_bits=7)
    lo = (mat - hi).astype(jnp.bfloat16)
    return hi.astype(jnp.bfloat16), lo


def dot_f32(a, b):
    return jnp.dot(a, b, preferred_element_type=jnp.float32)


def apply_bf16(rows, parts):
    hi, lo = parts
    return dot_f32(rows, hi) + dot_f32(rows, lo)


def apply_f32(rows, parts):
    hi, lo = parts
    rows_hi_f = lax.reduce_precision(rows, exponent_bits=8, mantissa_bits=7)
    rows_lo = (rows - rows_hi_f).astype(jnp.bfloat16)
    rows_hi = rows_hi_f.astype(jnp.bfloat16)
    return dot_f32(rows_hi, hi) + dot_f32(rows_hi, lo) + dot_f32(rows_lo, hi)


def pick(onehot, block):
    return jnp.einsum(
        "sb,nbc->nsc", onehot, block, preferred_element_type=jnp.float32
    ).astype(jnp.bfloat16)


def shards(
    orbitals,
    exchange_values,
    local_values,
    coupling,
    to_values_mat,
    to_coeffs_mat,
    laplace_blocks,
    box_counts,
    kept_mask,
    send_list,
    neighbour_pos,
):
    orb_dev, box_dev, width = orbitals.shape
    order_k = to_values_mat.shape[0]
    n_box = send_list.shape[1]
    rows = orb_dev * box_dev

    slots = send_list[0]
    box_ids = lax.iota(jnp.int32, box_dev)
    send_hot = (slots[:, None] == box_ids[None, :]).astype(jnp.bfloat16)
    outgoing = jnp.einsum(
        "sb,nbc->snc", send_hot, orbitals, preferred_element_type=jnp.float32
    ).astype(jnp.bfloat16)
    incoming = lax.all_to_all(outgoing, "box", split_axis=0, concat_axis=0, tiled=True)

    tv = to_values_mat.T
    values_t = split_bf16(kron3(tv, tv, tv))
    flat = orbitals.reshape(rows, width)
    values = apply_bf16(flat, values_t).reshape(orb_dev, box_dev, width)

    kept = kept_mask > 0
    rank = jnp.cumsum(kept.astype(jnp.int32)) - 1
    keep_ids = lax.iota(jnp.int32, KEEP)
    sel = kept[None, :] & (rank[None, :] == keep_ids[:, None])
    products = jnp.where(
        kept[None, :, None], exchange_values.astype(jnp.float32) * values, 0.0
    ).astype(jnp.bfloat16)
    compact = pick(sel.astype(jnp.bfloat16), products)
    gathered = lax.all_gather(
        compact.reshape(orb_dev, KEEP * width), "orb", axis=0, tiled=True
    )

    tc = to_coeffs_mat.T
    coeffs_t = split_bf16(kron3(tc, tc, tc))
    local_part = apply_f32((local_values[None, :, :] * values).reshape(rows, width), coeffs_t)

    lap0_t = laplace_blocks[0].T
    centre = sum(at_place(lap0_t, width, place) for place in range(3))
    kinetic = apply_bf16(flat, split_bf16(centre))
    faces = [at_place(laplace_blocks[1 + side].T, width, which)
             for which in range(3) for side in range(2)]
    face_hi, face_lo = split_bf16(jnp.stack(faces))
    face_pos = neighbour_pos.reshape(-1)
    local_hot = (face_pos[:, None] == box_ids[None, :]).astype(jnp.bfloat16)
    remote_ids = lax.iota(jnp.int32, n_box)
    remote_hot = ((face_pos[:, None] - box_dev) == remote_ids[None, :]).astype(jnp.bfloat16)
    moved = jnp.einsum(
        "gb,nbc->ngc", local_hot, orbitals, preferred_element_type=jnp.float32
    ) + jnp.einsum("gr,rnc->ngc", remote_hot, incoming, preferred_element_type=jnp.float32)
    moved = moved.astype(jnp.bfloat16).reshape(orb_dev, len(faces), box_dev, width)
    kinetic_faces = jnp.einsum(
        "nfbc,fcd->nbd", moved, face_hi, preferred_element_type=jnp.float32
    ) + jnp.einsum("nfbc,fcd->nbd", moved, face_lo, preferred_element_type=jnp.float32)
    kinetic = kinetic + kinetic_faces.reshape(rows, width)
    gathered, kinetic = lax.optimization_barrier((gathered, kinetic))

    mixed = dot_f32(coupling, gathered).reshape(orb_dev * KEEP, width)
    exchange_part = apply_f32(mixed, coeffs_t).reshape(orb_dev, KEEP, width)
    sel_f = sel.astype(jnp.float32)
    total = (local_part - 0.5 * kinetic).reshape(orb_dev, box_dev, width)
    for k in range(KEEP):
        total = total - exchange_part[:, k : k + 1, :] * sel_f[k][None, :, None]
    live = box_ids < box_counts[0]
    total = jnp.where(live[None, :, None], total, 0.0)
    return total.astype(jnp.bfloat16)


def solution(mesh):
    return jax.shard_map(
        shards,
        mesh=mesh,
        in_specs=(
            P("orb", "box", None),
            P("orb", "box", None),
            P("box", None),
            P("orb", None),
            P(),
            P(),
            P(),
            P("box"),
            P("box"),
            P("box", None),
            P(None, "box"),
        ),
        out_specs=P("orb", "box", None),
        check_vma=False,
    )
```

```python
import jax
import jax.numpy as jnp
from jax import lax
from jax.sharding import PartitionSpec as P

KEEP = 4


def digit_of(width, order_k, place):
    idx = lax.iota(jnp.int32, width)
    return (idx // (order_k ** (2 - place))) % order_k


def expand(mat, width, place):
    order_k = mat.shape[0]
    digit = digit_of(width, order_k, place)
    ks = lax.iota(jnp.int32, order_k)
    left = (digit[:, None] == ks[None, :]).astype(jnp.float32)
    right = (ks[:, None] == digit[None, :]).astype(jnp.float32)
    hp = lax.Precision.HIGHEST
    return jnp.dot(jnp.dot(left, mat, precision=hp), right, precision=hp)


def same_digit(width, order_k, place):
    digit = digit_of(width, order_k, place)
    return (digit[:, None] == digit[None, :]).astype(jnp.float32)


def kron3(a, b, c):
    width = a.shape[0] * b.shape[0] * c.shape[0]
    return expand(a, width, 0) * expand(b, width, 1) * expand(c, width, 2)


def at_place(mat, width, place):
    order_k = mat.shape[0]
    out = expand(mat, width, place)
    for other in range(3):
        if other != place:
            out = out * same_digit(width, order_k, other)
    return out


def split_bf16(mat):
    hi = lax.reduce_precision(mat, exponent_bits=8, mantissa_bits=7)
    lo = (mat - hi).astype(jnp.bfloat16)
    return hi.astype(jnp.bfloat16), lo


def dot_f32(a, b):
    return jnp.dot(a, b, preferred_element_type=jnp.float32)


def apply_bf16(rows, parts):
    hi, lo = parts
    return dot_f32(rows, hi) + dot_f32(rows, lo)


def apply_f32(rows, parts):
    hi, lo = parts
    rows_hi_f = lax.reduce_precision(rows, exponent_bits=8, mantissa_bits=7)
    rows_lo = (rows - rows_hi_f).astype(jnp.bfloat16)
    rows_hi = rows_hi_f.astype(jnp.bfloat16)
    return dot_f32(rows_hi, hi) + dot_f32(rows_hi, lo) + dot_f32(rows_lo, hi)


def pick(onehot, block):
    return jnp.einsum(
        "sb,nbc->nsc", onehot, block, preferred_element_type=jnp.float32
    ).astype(jnp.bfloat16)


def shards(
    orbitals,
    exchange_values,
    local_values,
    coupling,
    to_values_mat,
    to_coeffs_mat,
    laplace_blocks,
    box_counts,
    kept_mask,
    send_list,
    neighbour_pos,
):
    orb_dev, box_dev, width = orbitals.shape
    order_k = to_values_mat.shape[0]
    n_box = send_list.shape[1]
    rows = orb_dev * box_dev

    slots = send_list[0]
    box_ids = lax.iota(jnp.int32, box_dev)
    send_hot = (slots[:, None] == box_ids[None, :]).astype(jnp.bfloat16)
    outgoing = pick(send_hot, orbitals)
    half = orb_dev // 2
    incoming_a = lax.all_to_all(
        outgoing[:half], "box", split_axis=1, concat_axis=1, tiled=True
    )
    later, incoming_a = lax.optimization_barrier((outgoing[half:], incoming_a))
    incoming_b = lax.all_to_all(later, "box", split_axis=1, concat_axis=1, tiled=True)

    values_t = split_bf16(kron3(to_values_mat, to_values_mat, to_values_mat).T)
    flat = orbitals.reshape(rows, width)
    values = apply_bf16(flat, values_t).reshape(orb_dev, box_dev, width)

    kept = kept_mask > 0
    rank = jnp.cumsum(kept.astype(jnp.int32)) - 1
    keep_ids = lax.iota(jnp.int32, KEEP)
    sel = kept[None, :] & (rank[None, :] == keep_ids[:, None])
    products = jnp.where(
        kept[None, :, None], exchange_values.astype(jnp.float32) * values, 0.0
    ).astype(jnp.bfloat16)
    compact = pick(sel.astype(jnp.bfloat16), products)
    gathered = lax.all_gather(
        compact.reshape(orb_dev, KEEP * width), "orb", axis=0, tiled=True
    )
    lap0 = laplace_blocks[0]
    centre = sum(at_place(lap0, width, place) for place in range(3))
    kinetic = apply_bf16(flat, split_bf16(centre.T))
    faces = [at_place(laplace_blocks[1 + side], width, which).T
             for which in range(3) for side in range(2)]
    face_hi, face_lo = split_bf16(jnp.stack(faces))
    pool_ids = lax.iota(jnp.int32, box_dev + n_box)
    face_pos = neighbour_pos.reshape(-1)
    face_hot = (face_pos[:, None] == pool_ids[None, :]).astype(jnp.bfloat16)

    def face_part(own, arrived):
        pool = jnp.concatenate([own, arrived], axis=1)
        moved = pick(face_hot, pool).reshape(own.shape[0], len(faces), box_dev, width)
        return jnp.einsum(
            "nfbc,fcd->nbd", moved, face_hi, preferred_element_type=jnp.float32
        ) + jnp.einsum("nfbc,fcd->nbd", moved, face_lo, preferred_element_type=jnp.float32)

    first = face_part(orbitals[:half], incoming_a)
    gathered, first = lax.optimization_barrier((gathered, first))
    second = face_part(orbitals[half:], incoming_b)
    kinetic = kinetic + jnp.concatenate([first, second], axis=0).reshape(rows, width)
    mixed = dot_f32(coupling, gathered).reshape(orb_dev, KEEP, width)
    spread = jnp.take(mixed, jnp.clip(rank, 0, KEEP - 1), axis=1)
    exchange = jnp.where(kept[None, :, None], spread, 0.0)

    weighted = local_values[None, :, :] * values - exchange
    coeffs_t = split_bf16(kron3(to_coeffs_mat, to_coeffs_mat, to_coeffs_mat).T)
    potential = apply_f32(weighted.reshape(rows, width), coeffs_t)

    total = (potential - 0.5 * kinetic).reshape(orb_dev, box_dev, width)
    live = box_ids < box_counts[0]
    total = jnp.where(live[None, :, None], total, 0.0)
    return total.astype(jnp.bfloat16)


def solution(mesh):
    return jax.shard_map(
        shards,
        mesh=mesh,
        in_specs=(
            P("orb", "box", None),
            P("orb", "box", None),
            P("box", None),
            P("orb", None),
            P(),
            P(),
            P(),
            P("box"),
            P("box"),
            P("box", None),
            P(None, "box"),
        ),
        out_specs=P("orb", "box", None),
        check_vma=False,
    )
```

```python
import jax
import jax.numpy as jnp
from jax import lax
from jax.sharding import PartitionSpec as P

KEEP = 4


def digit_of(width, order_k, place):
    idx = lax.iota(jnp.int32, width)
    return (idx // (order_k ** (2 - place))) % order_k


def expand(mat, width, place):
    order_k = mat.shape[0]
    digit = digit_of(width, order_k, place)
    ks = lax.iota(jnp.int32, order_k)
    left = (digit[:, None] == ks[None, :]).astype(jnp.float32)
    right = (ks[:, None] == digit[None, :]).astype(jnp.float32)
    hp = lax.Precision.HIGHEST
    return jnp.dot(jnp.dot(left, mat, precision=hp), right, precision=hp)


def same_digit(width, order_k, place):
    digit = digit_of(width, order_k, place)
    return (digit[:, None] == digit[None, :]).astype(jnp.float32)


def kron3(a, b, c):
    width = a.shape[0] * b.shape[0] * c.shape[0]
    return expand(a, width, 0) * expand(b, width, 1) * expand(c, width, 2)


def at_place(mat, width, place):
    order_k = mat.shape[0]
    out = expand(mat, width, place)
    for other in range(3):
        if other != place:
            out = out * same_digit(width, order_k, other)
    return out


def split_bf16(mat):
    hi = lax.reduce_precision(mat, exponent_bits=8, mantissa_bits=7)
    lo = (mat - hi).astype(jnp.bfloat16)
    return hi.astype(jnp.bfloat16), lo


def dot_f32(a, b):
    return jnp.dot(a, b, preferred_element_type=jnp.float32)


def apply_bf16(rows, parts):
    hi, lo = parts
    return dot_f32(rows, hi) + dot_f32(rows, lo)


def apply_f32(rows, parts):
    hi, lo = parts
    rows_hi_f = lax.reduce_precision(rows, exponent_bits=8, mantissa_bits=7)
    rows_lo = (rows - rows_hi_f).astype(jnp.bfloat16)
    rows_hi = rows_hi_f.astype(jnp.bfloat16)
    return dot_f32(rows_hi, hi) + dot_f32(rows_hi, lo) + dot_f32(rows_lo, hi)


def pick(onehot, block):
    return jnp.einsum(
        "sb,nbc->nsc", onehot, block, preferred_element_type=jnp.float32
    ).astype(jnp.bfloat16)


def shards(
    orbitals,
    exchange_values,
    local_values,
    coupling,
    to_values_mat,
    to_coeffs_mat,
    laplace_blocks,
    box_counts,
    kept_mask,
    send_list,
    neighbour_pos,
):
    orb_dev, box_dev, width = orbitals.shape
    order_k = to_values_mat.shape[0]
    n_box = send_list.shape[1]
    rows = orb_dev * box_dev

    slots = send_list[0]
    box_ids = lax.iota(jnp.int32, box_dev)
    send_hot = (slots[:, None] == box_ids[None, :]).astype(jnp.bfloat16)
    outgoing = pick(send_hot, orbitals)
    half = (orb_dev * 2) // 3
    incoming_a = lax.all_to_all(
        outgoing[:half], "box", split_axis=1, concat_axis=1, tiled=True
    )
    later, incoming_a = lax.optimization_barrier((outgoing[half:], incoming_a))
    incoming_b = lax.all_to_all(later, "box", split_axis=1, concat_axis=1, tiled=True)

    values_t = split_bf16(kron3(to_values_mat, to_values_mat, to_values_mat).T)
    flat = orbitals.reshape(rows, width)
    values = apply_bf16(flat, values_t).reshape(orb_dev, box_dev, width)

    kept = kept_mask > 0
    rank = jnp.cumsum(kept.astype(jnp.int32)) - 1
    keep_ids = lax.iota(jnp.int32, KEEP)
    sel = kept[None, :] & (rank[None, :] == keep_ids[:, None])
    products = jnp.where(
        kept[None, :, None], exchange_values.astype(jnp.float32) * values, 0.0
    ).astype(jnp.bfloat16)
    compact = pick(sel.astype(jnp.bfloat16), products)
    gathered = lax.all_gather(
        compact.reshape(orb_dev, KEEP * width), "orb", axis=0, tiled=True
    )
    lap0 = laplace_blocks[0]
    centre = sum(at_place(lap0, width, place) for place in range(3))
    kinetic = apply_bf16(flat, split_bf16(centre.T))
    faces = [at_place(laplace_blocks[1 + side], width, which).T
             for which in range(3) for side in range(2)]
    face_hi, face_lo = split_bf16(jnp.stack(faces))
    pool_ids = lax.iota(jnp.int32, box_dev + n_box)
    face_pos = neighbour_pos.reshape(-1)
    face_hot = (face_pos[:, None] == pool_ids[None, :]).astype(jnp.bfloat16)

    def face_part(own, arrived):
        pool = jnp.concatenate([own, arrived], axis=1)
        moved = pick(face_hot, pool).reshape(own.shape[0], len(faces), box_dev, width)
        return jnp.einsum(
            "nfbc,fcd->nbd", moved, face_hi, preferred_element_type=jnp.float32
        ) + jnp.einsum("nfbc,fcd->nbd", moved, face_lo, preferred_element_type=jnp.float32)

    first = face_part(orbitals[:half], incoming_a)
    gathered, first = lax.optimization_barrier((gathered, first))
    mixed = dot_f32(coupling, gathered).reshape(orb_dev, KEEP, width)
    spread = jnp.take(mixed, jnp.clip(rank, 0, KEEP - 1), axis=1)
    exchange = jnp.where(kept[None, :, None], spread, 0.0)

    weighted = local_values[None, :, :] * values - exchange
    coeffs_t = split_bf16(kron3(to_coeffs_mat, to_coeffs_mat, to_coeffs_mat).T)
    potential = apply_f32(weighted.reshape(rows, width), coeffs_t)
    potential = potential.reshape(orb_dev, box_dev, width)
    kinetic = kinetic.reshape(orb_dev, box_dev, width)
    live = box_ids < box_counts[0]

    def finish(pot, kin):
        total = jnp.where(live[None, :, None], pot - 0.5 * kin, 0.0)
        return total.astype(jnp.bfloat16)

    head = finish(potential[:half], kinetic[:half] + first)
    head, incoming_b = lax.optimization_barrier((head, incoming_b))
    second = face_part(orbitals[half:], incoming_b)
    tail = finish(potential[half:], kinetic[half:] + second)
    return jnp.concatenate([head, tail], axis=0)


def solution(mesh):
    return jax.shard_map(
        shards,
        mesh=mesh,
        in_specs=(
            P("orb", "box", None),
            P("orb", "box", None),
            P("box", None),
            P("orb", None),
            P(),
            P(),
            P(),
            P("box"),
            P("box"),
            P("box", None),
            P(None, "box"),
        ),
        out_specs=P("orb", "box", None),
        check_vma=False,
    )
```

```python
import jax
import jax.numpy as jnp
from jax import lax
from jax.sharding import PartitionSpec as P

KEEP = 4


def digit_of(width, order_k, place):
    idx = lax.iota(jnp.int32, width)
    return (idx // (order_k ** (2 - place))) % order_k


def expand(mat, width, place):
    order_k = mat.shape[0]
    digit = digit_of(width, order_k, place)
    ks = lax.iota(jnp.int32, order_k)
    left = (digit[:, None] == ks[None, :]).astype(jnp.float32)
    right = (ks[:, None] == digit[None, :]).astype(jnp.float32)
    hp = lax.Precision.HIGHEST
    return jnp.dot(jnp.dot(left, mat, precision=hp), right, precision=hp)


def same_digit(width, order_k, place):
    digit = digit_of(width, order_k, place)
    return (digit[:, None] == digit[None, :]).astype(jnp.float32)


def kron3(a, b, c):
    width = a.shape[0] * b.shape[0] * c.shape[0]
    return expand(a, width, 0) * expand(b, width, 1) * expand(c, width, 2)


def at_place(mat, width, place):
    order_k = mat.shape[0]
    out = expand(mat, width, place)
    for other in range(3):
        if other != place:
            out = out * same_digit(width, order_k, other)
    return out


def split_bf16(mat):
    hi = lax.reduce_precision(mat, exponent_bits=8, mantissa_bits=7)
    lo = (mat - hi).astype(jnp.bfloat16)
    return hi.astype(jnp.bfloat16), lo


def dot_f32(a, b):
    return jnp.dot(a, b, preferred_element_type=jnp.float32)


def apply_bf16(rows, parts):
    hi, lo = parts
    return dot_f32(rows, hi) + dot_f32(rows, lo)


def apply_f32(rows, parts):
    hi, lo = parts
    rows_hi_f = lax.reduce_precision(rows, exponent_bits=8, mantissa_bits=7)
    rows_lo = (rows - rows_hi_f).astype(jnp.bfloat16)
    rows_hi = rows_hi_f.astype(jnp.bfloat16)
    return dot_f32(rows_hi, hi) + dot_f32(rows_hi, lo) + dot_f32(rows_lo, hi)


def pick(onehot, block):
    return jnp.einsum(
        "sb,nbc->nsc", onehot, block, preferred_element_type=jnp.float32
    ).astype(jnp.bfloat16)


def shards(
    orbitals,
    exchange_values,
    local_values,
    coupling,
    to_values_mat,
    to_coeffs_mat,
    laplace_blocks,
    box_counts,
    kept_mask,
    send_list,
    neighbour_pos,
):
    orb_dev, box_dev, width = orbitals.shape
    order_k = to_values_mat.shape[0]
    n_box = send_list.shape[1]
    rows = orb_dev * box_dev

    slots = send_list[0]
    box_ids = lax.iota(jnp.int32, box_dev)
    send_hot = (slots[:, None] == box_ids[None, :]).astype(jnp.bfloat16)
    outgoing = pick(send_hot, orbitals)
    half = (orb_dev * 2) // 3
    incoming_a = lax.all_to_all(
        outgoing[:half], "box", split_axis=1, concat_axis=1, tiled=True
    )
    later, incoming_a = lax.optimization_barrier((outgoing[half:], incoming_a))
    incoming_b = lax.all_to_all(later, "box", split_axis=1, concat_axis=1, tiled=True)

    values_t = split_bf16(kron3(to_values_mat, to_values_mat, to_values_mat).T)
    flat = orbitals.reshape(rows, width)
    values = apply_bf16(flat, values_t).reshape(orb_dev, box_dev, width)

    kept = kept_mask > 0
    rank = jnp.cumsum(kept.astype(jnp.int32)) - 1
    keep_ids = lax.iota(jnp.int32, KEEP)
    sel = kept[None, :] & (rank[None, :] == keep_ids[:, None])
    products = jnp.where(
        kept[None, :, None], exchange_values.astype(jnp.float32) * values, 0.0
    ).astype(jnp.bfloat16)
    compact = pick(sel.astype(jnp.bfloat16), products)
    n_orb = coupling.shape[1] // orb_dev
    chips = n_orb // 2
    same_core = [[chip * 2 + core for chip in range(chips)] for core in range(2)]
    mates = [[chip * 2, chip * 2 + 1] for chip in range(chips)]
    across = lax.all_gather(
        compact.reshape(orb_dev, KEEP * width), "orb", axis=0,
        axis_index_groups=same_core,
    )
    both = lax.all_gather(across, "orb", axis=0, axis_index_groups=mates)
    gathered = both.reshape(n_orb * orb_dev, KEEP * width)
    coupling = coupling.reshape(orb_dev, chips, 2, orb_dev).transpose(0, 2, 1, 3)
    coupling = coupling.reshape(orb_dev, n_orb * orb_dev)
    lap0 = laplace_blocks[0]
    centre = sum(at_place(lap0, width, place) for place in range(3))
    kinetic = apply_bf16(flat, split_bf16(centre.T))
    faces = [at_place(laplace_blocks[1 + side], width, which).T
             for which in range(3) for side in range(2)]
    face_hi, face_lo = split_bf16(jnp.stack(faces))
    pool_ids = lax.iota(jnp.int32, box_dev + n_box)
    face_pos = neighbour_pos.reshape(-1)
    face_hot = (face_pos[:, None] == pool_ids[None, :]).astype(jnp.bfloat16)

    def face_part(own, arrived):
        pool = jnp.concatenate([own, arrived], axis=1)
        moved = pick(face_hot, pool).reshape(own.shape[0], len(faces), box_dev, width)
        return jnp.einsum(
            "nfbc,fcd->nbd", moved, face_hi, preferred_element_type=jnp.float32
        ) + jnp.einsum("nfbc,fcd->nbd", moved, face_lo, preferred_element_type=jnp.float32)

    first = face_part(orbitals[:half], incoming_a)
    gathered, first = lax.optimization_barrier((gathered, first))
    mixed = dot_f32(coupling, gathered).reshape(orb_dev, KEEP, width)
    spread = jnp.take(mixed, jnp.clip(rank, 0, KEEP - 1), axis=1)
    exchange = jnp.where(kept[None, :, None], spread, 0.0)

    weighted = local_values[None, :, :] * values - exchange
    coeffs_t = split_bf16(kron3(to_coeffs_mat, to_coeffs_mat, to_coeffs_mat).T)
    potential = apply_f32(weighted.reshape(rows, width), coeffs_t)
    potential = potential.reshape(orb_dev, box_dev, width)
    kinetic = kinetic.reshape(orb_dev, box_dev, width)
    live = box_ids < box_counts[0]

    def finish(pot, kin):
        total = jnp.where(live[None, :, None], pot - 0.5 * kin, 0.0)
        return total.astype(jnp.bfloat16)

    head = finish(potential[:half], kinetic[:half] + first)
    head, incoming_b = lax.optimization_barrier((head, incoming_b))
    second = face_part(orbitals[half:], incoming_b)
    tail = finish(potential[half:], kinetic[half:] + second)
    return jnp.concatenate([head, tail], axis=0)


def solution(mesh):
    return jax.shard_map(
        shards,
        mesh=mesh,
        in_specs=(
            P("orb", "box", None),
            P("orb", "box", None),
            P("box", None),
            P("orb", None),
            P(),
            P(),
            P(),
            P("box"),
            P("box"),
            P("box", None),
            P(None, "box"),
        ),
        out_specs=P("orb", "box", None),
        check_vma=False,
    )
```

```python
import jax
import jax.numpy as jnp
from jax import lax
from jax.sharding import PartitionSpec as P

KEEP = 4


def digit_of(width, order_k, place):
    idx = lax.iota(jnp.int32, width)
    return (idx // (order_k ** (2 - place))) % order_k


def expand(mat, width, place):
    order_k = mat.shape[0]
    digit = digit_of(width, order_k, place)
    ks = lax.iota(jnp.int32, order_k)
    left = (digit[:, None] == ks[None, :]).astype(jnp.float32)
    right = (ks[:, None] == digit[None, :]).astype(jnp.float32)
    hp = lax.Precision.HIGHEST
    return jnp.dot(jnp.dot(left, mat, precision=hp), right, precision=hp)


def same_digit(width, order_k, place):
    digit = digit_of(width, order_k, place)
    return (digit[:, None] == digit[None, :]).astype(jnp.float32)


def kron3(a, b, c):
    width = a.shape[0] * b.shape[0] * c.shape[0]
    return expand(a, width, 0) * expand(b, width, 1) * expand(c, width, 2)


def at_place(mat, width, place):
    order_k = mat.shape[0]
    out = expand(mat, width, place)
    for other in range(3):
        if other != place:
            out = out * same_digit(width, order_k, other)
    return out


def split_bf16(mat):
    hi = lax.reduce_precision(mat, exponent_bits=8, mantissa_bits=7)
    lo = (mat - hi).astype(jnp.bfloat16)
    return hi.astype(jnp.bfloat16), lo


def dot_f32(a, b):
    return jnp.dot(a, b, preferred_element_type=jnp.float32)


def apply_bf16(rows, parts):
    hi, lo = parts
    return dot_f32(rows, hi) + dot_f32(rows, lo)


def apply_f32(rows, parts):
    hi, lo = parts
    rows_hi_f = lax.reduce_precision(rows, exponent_bits=8, mantissa_bits=7)
    rows_lo = (rows - rows_hi_f).astype(jnp.bfloat16)
    rows_hi = rows_hi_f.astype(jnp.bfloat16)
    return dot_f32(rows_hi, hi) + dot_f32(rows_hi, lo) + dot_f32(rows_lo, hi)


def pick(onehot, block):
    return jnp.einsum(
        "sb,nbc->nsc", onehot, block, preferred_element_type=jnp.float32
    ).astype(jnp.bfloat16)


def shards(
    orbitals,
    exchange_values,
    local_values,
    coupling,
    to_values_mat,
    to_coeffs_mat,
    laplace_blocks,
    box_counts,
    kept_mask,
    send_list,
    neighbour_pos,
):
    orb_dev, box_dev, width = orbitals.shape
    order_k = to_values_mat.shape[0]
    n_box = send_list.shape[1]
    rows = orb_dev * box_dev

    slots = send_list[0]
    box_ids = lax.iota(jnp.int32, box_dev)
    send_hot = (slots[:, None] == box_ids[None, :]).astype(jnp.bfloat16)
    outgoing = pick(send_hot, orbitals)
    half = (orb_dev * 7) // 12
    incoming_a = lax.all_to_all(
        outgoing[:half], "box", split_axis=1, concat_axis=1, tiled=True
    )
    later, incoming_a = lax.optimization_barrier((outgoing[half:], incoming_a))
    incoming_b = lax.all_to_all(later, "box", split_axis=1, concat_axis=1, tiled=True)

    values_t = split_bf16(kron3(to_values_mat, to_values_mat, to_values_mat).T)
    flat = orbitals.reshape(rows, width)
    values = apply_bf16(flat, values_t).reshape(orb_dev, box_dev, width)

    kept = kept_mask > 0
    rank = jnp.cumsum(kept.astype(jnp.int32)) - 1
    keep_ids = lax.iota(jnp.int32, KEEP)
    sel = kept[None, :] & (rank[None, :] == keep_ids[:, None])
    products = jnp.where(
        kept[None, :, None], exchange_values.astype(jnp.float32) * values, 0.0
    ).astype(jnp.bfloat16)
    compact = pick(sel.astype(jnp.bfloat16), products)
    gathered = lax.all_gather(
        compact.reshape(orb_dev, KEEP * width), "orb", axis=0, tiled=True
    )
    lap0 = laplace_blocks[0]
    centre = sum(at_place(lap0, width, place) for place in range(3))
    kinetic = apply_bf16(flat, split_bf16(centre.T))
    faces = [at_place(laplace_blocks[1 + side], width, which).T
             for which in range(3) for side in range(2)]
    face_hi, face_lo = split_bf16(jnp.stack(faces))
    pool_ids = lax.iota(jnp.int32, box_dev + n_box)
    face_pos = neighbour_pos.reshape(-1)
    face_hot = (face_pos[:, None] == pool_ids[None, :]).astype(jnp.bfloat16)

    def face_part(own, arrived):
        pool = jnp.concatenate([own, arrived], axis=1)
        moved = pick(face_hot, pool).reshape(own.shape[0], len(faces), box_dev, width)
        return jnp.einsum(
            "nfbc,fcd->nbd", moved, face_hi, preferred_element_type=jnp.float32
        ) + jnp.einsum("nfbc,fcd->nbd", moved, face_lo, preferred_element_type=jnp.float32)

    first = face_part(orbitals[:half], incoming_a)
    gathered, first = lax.optimization_barrier((gathered, first))
    mixed = dot_f32(coupling, gathered).reshape(orb_dev, KEEP, width)
    spread = jnp.take(mixed, jnp.clip(rank, 0, KEEP - 1), axis=1)
    exchange = jnp.where(kept[None, :, None], spread, 0.0)

    weighted = local_values[None, :, :] * values - exchange
    coeffs_t = split_bf16(kron3(to_coeffs_mat, to_coeffs_mat, to_coeffs_mat).T)
    potential = apply_f32(weighted.reshape(rows, width), coeffs_t)
    potential = potential.reshape(orb_dev, box_dev, width)
    kinetic = kinetic.reshape(orb_dev, box_dev, width)
    live = box_ids < box_counts[0]

    def finish(pot, kin):
        total = jnp.where(live[None, :, None], pot - 0.5 * kin, 0.0)
        return total.astype(jnp.bfloat16)

    head = finish(potential[:half], kinetic[:half] + first)
    head, incoming_b = lax.optimization_barrier((head, incoming_b))
    second = face_part(orbitals[half:], incoming_b)
    tail = finish(potential[half:], kinetic[half:] + second)
    return jnp.concatenate([head, tail], axis=0)


def solution(mesh):
    return jax.shard_map(
        shards,
        mesh=mesh,
        in_specs=(
            P("orb", "box", None),
            P("orb", "box", None),
            P("box", None),
            P("orb", None),
            P(),
            P(),
            P(),
            P("box"),
            P("box"),
            P("box", None),
            P(None, "box"),
        ),
        out_specs=P("orb", "box", None),
        check_vma=False,
    )
```

```python
import jax
import jax.numpy as jnp
from jax import lax
from jax.sharding import PartitionSpec as P

KEEP = 4


def digit_of(width, order_k, place):
    idx = lax.iota(jnp.int32, width)
    return (idx // (order_k ** (2 - place))) % order_k


def expand(mat, width, place):
    order_k = mat.shape[0]
    digit = digit_of(width, order_k, place)
    ks = lax.iota(jnp.int32, order_k)
    left = (digit[:, None] == ks[None, :]).astype(jnp.float32)
    right = (ks[:, None] == digit[None, :]).astype(jnp.float32)
    hp = lax.Precision.HIGHEST
    return jnp.dot(jnp.dot(left, mat, precision=hp), right, precision=hp)


def same_digit(width, order_k, place):
    digit = digit_of(width, order_k, place)
    return (digit[:, None] == digit[None, :]).astype(jnp.float32)


def kron3(a, b, c):
    width = a.shape[0] * b.shape[0] * c.shape[0]
    return expand(a, width, 0) * expand(b, width, 1) * expand(c, width, 2)


def at_place(mat, width, place):
    order_k = mat.shape[0]
    out = expand(mat, width, place)
    for other in range(3):
        if other != place:
            out = out * same_digit(width, order_k, other)
    return out


def split_bf16(mat):
    hi = lax.reduce_precision(mat, exponent_bits=8, mantissa_bits=7)
    lo = (mat - hi).astype(jnp.bfloat16)
    return hi.astype(jnp.bfloat16), lo


def dot_f32(a, b):
    return jnp.dot(a, b, preferred_element_type=jnp.float32)


def apply_bf16(rows, parts):
    hi, lo = parts
    return dot_f32(rows, hi) + dot_f32(rows, lo)


def apply_f32(rows, parts):
    hi, lo = parts
    rows_hi_f = lax.reduce_precision(rows, exponent_bits=8, mantissa_bits=7)
    rows_lo = (rows - rows_hi_f).astype(jnp.bfloat16)
    rows_hi = rows_hi_f.astype(jnp.bfloat16)
    return dot_f32(rows_hi, hi) + dot_f32(rows_hi, lo) + dot_f32(rows_lo, hi)


def pick(onehot, block):
    return jnp.einsum(
        "sb,nbc->nsc", onehot, block, preferred_element_type=jnp.float32
    ).astype(jnp.bfloat16)


def shards(
    orbitals,
    exchange_values,
    local_values,
    coupling,
    to_values_mat,
    to_coeffs_mat,
    laplace_blocks,
    box_counts,
    kept_mask,
    send_list,
    neighbour_pos,
):
    orb_dev, box_dev, width = orbitals.shape
    order_k = to_values_mat.shape[0]
    n_box = send_list.shape[1]
    rows = orb_dev * box_dev

    slots = send_list[0]
    box_ids = lax.iota(jnp.int32, box_dev)
    send_hot = (slots[:, None] == box_ids[None, :]).astype(jnp.bfloat16)
    outgoing = pick(send_hot, orbitals)
    half = orb_dev // 2
    incoming_a = lax.all_to_all(
        outgoing[:half], "box", split_axis=1, concat_axis=1, tiled=True
    )
    later, incoming_a = lax.optimization_barrier((outgoing[half:], incoming_a))
    incoming_b = lax.all_to_all(later, "box", split_axis=1, concat_axis=1, tiled=True)

    values_t = split_bf16(kron3(to_values_mat, to_values_mat, to_values_mat).T)
    flat = orbitals.reshape(rows, width)
    values = apply_bf16(flat, values_t).reshape(orb_dev, box_dev, width)

    kept = kept_mask > 0
    rank = jnp.cumsum(kept.astype(jnp.int32)) - 1
    keep_ids = lax.iota(jnp.int32, KEEP)
    sel = kept[None, :] & (rank[None, :] == keep_ids[:, None])
    products = jnp.where(
        kept[None, :, None], exchange_values.astype(jnp.float32) * values, 0.0
    ).astype(jnp.bfloat16)
    compact = pick(sel.astype(jnp.bfloat16), products)
    gathered = lax.all_gather(
        compact.reshape(orb_dev, KEEP * width), "orb", axis=0, tiled=True
    )
    lap0 = laplace_blocks[0]
    centre = sum(at_place(lap0, width, place) for place in range(3))
    kinetic = apply_bf16(flat, split_bf16(centre.T))
    faces = [at_place(laplace_blocks[1 + side], width, which).T
             for which in range(3) for side in range(2)]
    face_hi, face_lo = split_bf16(jnp.stack(faces))
    pool_ids = lax.iota(jnp.int32, box_dev + n_box)
    face_pos = neighbour_pos.reshape(-1)
    face_hot = (face_pos[:, None] == pool_ids[None, :]).astype(jnp.bfloat16)

    def face_part(own, arrived):
        pool = jnp.concatenate([own, arrived], axis=1)
        moved = pick(face_hot, pool).reshape(own.shape[0], len(faces), box_dev, width)
        return jnp.einsum(
            "nfbc,fcd->nbd", moved, face_hi, preferred_element_type=jnp.float32
        ) + jnp.einsum("nfbc,fcd->nbd", moved, face_lo, preferred_element_type=jnp.float32)

    first = face_part(orbitals[:half], incoming_a)
    gathered, first = lax.optimization_barrier((gathered, first))
    mixed = dot_f32(coupling, gathered).reshape(orb_dev, KEEP, width)
    spread = jnp.take(mixed, jnp.clip(rank, 0, KEEP - 1), axis=1)
    exchange = jnp.where(kept[None, :, None], spread, 0.0)

    weighted = local_values[None, :, :] * values - exchange
    coeffs_t = split_bf16(kron3(to_coeffs_mat, to_coeffs_mat, to_coeffs_mat).T)
    potential = apply_f32(weighted.reshape(rows, width), coeffs_t)
    potential = potential.reshape(orb_dev, box_dev, width)
    kinetic = kinetic.reshape(orb_dev, box_dev, width)
    live = box_ids < box_counts[0]

    def finish(pot, kin):
        total = jnp.where(live[None, :, None], pot - 0.5 * kin, 0.0)
        return total.astype(jnp.bfloat16)

    head = finish(potential[:half], kinetic[:half] + first)
    head, incoming_b = lax.optimization_barrier((head, incoming_b))
    second = face_part(orbitals[half:], incoming_b)
    tail = finish(potential[half:], kinetic[half:] + second)
    return jnp.concatenate([head, tail], axis=0)


def solution(mesh):
    return jax.shard_map(
        shards,
        mesh=mesh,
        in_specs=(
            P("orb", "box", None),
            P("orb", "box", None),
            P("box", None),
            P("orb", None),
            P(),
            P(),
            P(),
            P("box"),
            P("box"),
            P("box", None),
            P(None, "box"),
        ),
        out_specs=P("orb", "box", None),
        check_vma=False,
    )
```
